128 devices in a mesh: inp: 8 (over z_lo, y), wide: 16 (over z_hi, x, core).
Axes of the slice: x: 4, y: 4, z: 4 (z_hi: 2, z_lo: 2; z = z_hi * 2 + z_lo), core: 2. Of those that a mesh axis runs over, the one named last changes fastest.
Arguments:
- voltages: int32 [1280, 196608], P('inp', 'wide'), may hold values from -8 to 7
- prototype: float32 [4, 4096], replicated, may hold values from -0.75 to 0.75
- input_gain: float32 [1280], P('inp'), may hold values from 0.5 to 1.5
- usable: int32 [1280], P('inp'), may hold values 0 or 1
Outputs:
- visibility: float32 [2, 128, 1280, 1280], P(None, 'wide', 'inp')
The draws below stay inside these ranges and needn't reach their ends.
All inputs are finite; a program needn't handle non-finite values. No bound on the sum of `usable` on one device may be relied on, other than what follows from the above.
Results may differ from the reference program's by a relative error of at most 0.0035.
Values may be sent and summed in bfloat16 or wider, within the bound.
No kernel may reach another device: no remote copies, remote signals or barrier semaphores. Data moves between devices by JAX's collectives and lax.ppermute only.
A program may use at most 192 MiB of HBM per device.

```python
import math
import jax
import jax.numpy as jnp
from jax import lax

CH = 2048
SPAN = 4096
TAPS = 4
AVG = 16
INP_DEV = 160
FR_DEV = 3
NI = 1280
FRAMES = 48
SAMPLES = 196608
GROUPS = 128
N_INP = 8


def place_ends(drawn, stream_key, smallest, top_value):
    shape = drawn.shape
    index_at = [jax.random.randint(jax.random.fold_in(stream_key, axis), (), 0, shape[axis]) for axis in range(len(shape))]
    drawn = drawn.at[tuple(index_at)].set(smallest)
    longest = shape.index(max(shape))
    index_at[longest] = (index_at[longest] + 1) % shape[longest]
    return drawn.at[tuple(index_at)].set(top_value)


def block_levels(own_key, dims, pieces, smallest, top_value):
    def one(axis_at, parts):
        steps = jax.random.uniform(jax.random.fold_in(jax.random.fold_in(own_key, 6), axis_at), (parts,), jnp.float32, smallest / len(pieces), top_value / len(pieces))
        return jnp.repeat(jnp.exp(steps), dims[axis_at] // parts).reshape((-1,) + (1,) * (len(dims) - axis_at - 1))

    factor_of = one(*pieces[0])
    for cut in pieces[1:]:
        factor_of = factor_of * one(*cut)
    return factor_of


def noise(stream_key, extent, spread, most, held_as=jnp.bfloat16):
    values = jax.random.normal(stream_key, extent, jnp.float32) * spread
    return jnp.minimum(jnp.maximum(values, -most), most).astype(held_as)


def setup_inputs(seed: int = 0) -> dict:
    keys = jax.random.split(jax.random.key(seed), 5)
    return {
        "voltages": place_ends(jax.random.randint(keys[0], (NI, SAMPLES), -8, 8), jax.random.fold_in(keys[0], 1), -8, 7).astype(jnp.int32),
        "prototype": noise(keys[1], (TAPS, SPAN), 0.125, 0.75, jnp.float32),
        "input_gain": jnp.clip(jnp.exp(math.log(1.5) - 1.0986123 * jax.random.uniform(keys[2], (NI,), jnp.float32) ** block_levels(keys[2], (NI,), ((0, 8),), -0.2, 0.2)), 0.5, 1.5),
        "usable": place_ends((jax.random.randint(keys[3], (NI,), 0, 8) < 7).astype(jnp.int32), jax.random.fold_in(keys[3], 1), 0, 1),
    }


def channelize(voltages, prototype, input_gain, usable):

    def one_block(packed):
        volts_rows, gain_rows, usable_rows = packed
        members = volts_rows.shape[0]
        samples = volts_rows.astype(jnp.float32).reshape(members, FRAMES, SPAN)
        padded = jnp.pad(samples, ((0, 0), (TAPS - 1, 0), (0, 0)))
        position = jnp.arange(FRAMES, dtype=jnp.int32) % FR_DEV
        near_sum = jnp.zeros(samples.shape, jnp.float32)
        far_sum = jnp.zeros(samples.shape, jnp.float32)
        for tap_index in range(TAPS):
            first_frame = TAPS - 1 - tap_index
            tap_term = prototype[tap_index][None, None, :] * padded[:, first_frame:first_frame + FRAMES, :]
            inside = (position >= tap_index)[None, :, None]
            near_sum = near_sum + jnp.where(inside, tap_term, 0.0)
            far_sum = far_sum + jnp.where(inside, 0.0, tap_term)
        far_sent = lax.optimization_barrier(far_sum.astype(jnp.bfloat16)).astype(jnp.float32)
        filtered = near_sum + far_sent
        spectrum = jnp.fft.rfft(filtered, axis=-1)[:, :, :CH]
        factor = (gain_rows * usable_rows.astype(jnp.float32) / math.sqrt(SPAN))[:, None, None]
        real_part = (jnp.real(spectrum) * factor).astype(jnp.bfloat16)
        imag_part = (jnp.imag(spectrum) * factor).astype(jnp.bfloat16)
        return jnp.stack([real_part, imag_part])
    blocks = lax.map(one_block, (voltages.reshape(N_INP, INP_DEV, SAMPLES), input_gain.reshape(N_INP, INP_DEV), usable.reshape(N_INP, INP_DEV)))
    return jnp.transpose(blocks, (1, 0, 2, 3, 4)).reshape(2, NI, FRAMES, CH)

def correlate(spectra):
    grouped = spectra.reshape(2, NI, FRAMES, GROUPS, AVG)
    grouped = jnp.transpose(grouped, (3, 0, 1, 2, 4))
    normalize = 1.0 / math.sqrt(AVG * FRAMES)

    def one_group(values):
        wide_values = values.astype(jnp.float32)
        products = jnp.einsum('pafc,qbfc->pqab', wide_values, wide_values, precision=lax.Precision.HIGHEST)
        real_part = products[0, 0] + products[1, 1]
        imag_part = products[1, 0] - products[0, 1]
        return jnp.stack([real_part, imag_part]) * normalize
    return jnp.transpose(lax.map(one_group, grouped), (1, 0, 2, 3))

def reference(voltages, prototype, input_gain, usable):
    return correlate(channelize(voltages, prototype, input_gain, usable))
```

```python
import math

import jax
import jax.numpy as jnp
from jax import lax
from jax.sharding import PartitionSpec as P

AVG = 16


def passed_along(value, axis, steps):
    count = lax.axis_size(axis)
    initial, last = (max(0, -steps), min(count, count - steps))
    return lax.ppermute(value, axis, [(source, source + steps) for source in range(initial, last)])


def phase_tables(rows_count, cols_count, modulus):
    first_index = jnp.arange(rows_count, dtype=jnp.int32)[:, None]
    second_index = jnp.arange(cols_count, dtype=jnp.int32)[None, :]
    angle = (first_index * second_index % modulus).astype(jnp.float32) * (2.0 * math.pi / modulus)
    return (jnp.cos(angle), jnp.sin(angle))


def transform(filtered, channels):
    total_rows, span_len = filtered.shape
    inner_len = min(span_len, 128)
    outer_len = span_len // inner_len
    kept_count = channels // outer_len
    highest = lax.Precision.HIGHEST
    reshaped = filtered.reshape(total_rows, outer_len, inner_len)
    cos_one, sin_one = phase_tables(outer_len, outer_len, outer_len)
    section_real = jnp.einsum("ran,ak->rkn", reshaped, cos_one, precision=highest)
    section_imag = -jnp.einsum("ran,ak->rkn", reshaped, sin_one, precision=highest)
    cos_two, sin_two = phase_tables(outer_len, inner_len, span_len)
    turned_real = section_real * cos_two + section_imag * sin_two
    turned_imag = section_imag * cos_two - section_real * sin_two
    cos_three, sin_three = phase_tables(inner_len, kept_count, inner_len)
    real_out = jnp.einsum("rkn,nm->rmk", turned_real, cos_three, precision=highest) + jnp.einsum(
        "rkn,nm->rmk", turned_imag, sin_three, precision=highest
    )
    imag_out = jnp.einsum("rkn,nm->rmk", turned_imag, cos_three, precision=highest) - jnp.einsum(
        "rkn,nm->rmk", turned_real, sin_three, precision=highest
    )
    return (real_out.reshape(total_rows, channels), imag_out.reshape(total_rows, channels))


def channelize(voltages, prototype, input_gain, usable):
    members, width_all = voltages.shape
    taps_count, span_len = prototype.shape
    frames_own = width_all // span_len
    channels = span_len // 2
    samples = voltages.astype(jnp.float32).reshape(members, frames_own, span_len)
    near_sum = jnp.zeros(samples.shape, jnp.float32)
    for tap_index in range(taps_count):
        delayed = jnp.pad(samples[:, : frames_own - tap_index], ((0, 0), (tap_index, 0), (0, 0)))
        near_sum = near_sum + prototype[tap_index][None, None, :] * delayed
    edge_parts = []
    for frame_index in range(taps_count - 1):
        partial_sum = jnp.zeros((members, span_len), jnp.float32)
        for tap_index in range(frame_index + 1, taps_count):
            partial_sum = (
                partial_sum
                + prototype[tap_index][None, :] * samples[:, frames_own + frame_index - tap_index]
            )
        edge_parts.append(partial_sum)
    outgoing = jnp.stack(edge_parts, axis=1).astype(jnp.bfloat16)
    incoming = passed_along(outgoing, "wide", 1).astype(jnp.float32)
    filtered = jnp.concatenate([near_sum + incoming, near_sum[:, taps_count - 1 :]], axis=1)
    real_out, imag_out = transform(filtered.reshape(members * frames_own, span_len), channels)
    factor = (input_gain * usable.astype(jnp.float32) / math.sqrt(span_len))[:, None, None]
    return jnp.stack(
        [
            real_out.reshape(members, frames_own, channels) * factor,
            imag_out.reshape(members, frames_own, channels) * factor,
        ]
    ).astype(jnp.bfloat16)


def shards(voltages, prototype, input_gain, usable):
    spectra = channelize(voltages, prototype, input_gain, usable)
    _, members, frames_own, channels = spectra.shape
    n_inp = lax.axis_size("inp")
    n_wide = lax.axis_size("wide")
    n_dev = n_inp * n_wide
    group_width = channels // n_dev
    chunks = spectra.reshape(2, members, frames_own, n_dev, group_width).transpose(3, 0, 1, 2, 4)
    arrived = lax.all_to_all(chunks, ("wide", "inp"), 0, 0, tiled=True)
    arrived = arrived.reshape(n_wide, n_inp, 2, members, frames_own, group_width)
    every = arrived.transpose(2, 1, 3, 0, 4, 5).reshape(2, n_inp * members, n_wide * frames_own * group_width)
    real_part, imag_part = every[0], every[1]
    left = jnp.stack(
        [jnp.concatenate([real_part, imag_part], axis=1), jnp.concatenate([imag_part, -real_part], axis=1)]
    )
    right = jnp.concatenate([real_part, imag_part], axis=1)
    normalize = 1.0 / math.sqrt(n_wide * frames_own * AVG)
    left = left.reshape(2, n_inp, members, left.shape[-1])
    products = jnp.einsum("pjak,bk->jpab", left, right, preferred_element_type=jnp.float32) * normalize
    spread = lax.all_to_all(products, "inp", 0, 0, tiled=True)
    return spread.transpose(1, 0, 2, 3)


def solution(mesh):
    return jax.shard_map(
        shards,
        mesh=mesh,
        in_specs=(P("inp", "wide"), P(), P("inp"), P("inp")),
        out_specs=P(None, "wide", "inp", None),
        check_vma=False,
    )
```

```python
import math

import jax
import jax.numpy as jnp
from jax import lax
from jax.sharding import PartitionSpec as P

AVG = 16


def passed_along(value, axis, steps):
    count = lax.axis_size(axis)
    initial, last = (max(0, -steps), min(count, count - steps))
    return lax.ppermute(value, axis, [(source, source + steps) for source in range(initial, last)])


def phase_tables(rows_count, cols_count, modulus):
    first_index = jnp.arange(rows_count, dtype=jnp.int32)[:, None]
    second_index = jnp.arange(cols_count, dtype=jnp.int32)[None, :]
    angle = (first_index * second_index % modulus).astype(jnp.float32) * (2.0 * math.pi / modulus)
    return (jnp.cos(angle), jnp.sin(angle))


def filter_frames(voltages, prototype):
    members, width_all = voltages.shape
    taps_count, span_len = prototype.shape
    frames_own = width_all // span_len
    samples = [voltages[:, f * span_len : (f + 1) * span_len].astype(jnp.float32) for f in range(frames_own)]
    near = []
    for f in range(frames_own):
        total = prototype[0][None, :] * samples[f]
        for tap_index in range(1, min(f, taps_count - 1) + 1):
            total = total + prototype[tap_index][None, :] * samples[f - tap_index]
        near.append(total)
    edge_parts = []
    for frame_index in range(taps_count - 1):
        partial_sum = jnp.zeros((members, span_len), jnp.float32)
        for tap_index in range(frame_index + 1, taps_count):
            partial_sum = partial_sum + prototype[tap_index][None, :] * samples[frames_own + frame_index - tap_index]
        edge_parts.append(partial_sum)
    outgoing = jnp.stack(edge_parts).astype(jnp.bfloat16)
    incoming = passed_along(outgoing, "wide", 1).astype(jnp.float32)
    rows = [near[f] + incoming[f] if f < taps_count - 1 else near[f] for f in range(frames_own)]
    return jnp.stack(rows)


def channelize(voltages, prototype, input_gain, usable):
    members = voltages.shape[0]
    span_len = prototype.shape[1]
    channels = span_len // 2
    filtered = filter_frames(voltages, prototype)
    frames_own = filtered.shape[0]
    rows = frames_own * members
    inner_len = min(span_len, 128)
    outer_len = span_len // inner_len
    kept_count = channels // outer_len
    highest = lax.Precision.HIGHEST
    shaped = filtered.reshape(rows, outer_len, inner_len)
    cos_one, sin_one = phase_tables(outer_len, outer_len, outer_len)
    first = jnp.concatenate([cos_one, -sin_one], axis=0)
    stage = jnp.einsum("ka,ran->krn", first, shaped, precision=highest)
    stage_real, stage_imag = stage[:outer_len], stage[outer_len:]
    cos_two, sin_two = phase_tables(outer_len, inner_len, span_len)
    turned_real = stage_real * cos_two[:, None, :] + stage_imag * sin_two[:, None, :]
    turned_imag = stage_imag * cos_two[:, None, :] - stage_real * sin_two[:, None, :]
    turned = jnp.concatenate([turned_real, turned_imag], axis=2)
    cos_three, sin_three = phase_tables(kept_count, inner_len, inner_len)
    second = jnp.concatenate(
        [jnp.concatenate([cos_three, sin_three], axis=1), jnp.concatenate([-sin_three, cos_three], axis=1)], axis=0
    )
    out = jnp.einsum("mn,krn->mkr", second, turned, precision=highest)
    out = out.reshape(2, channels, frames_own, members)
    factor = input_gain * usable.astype(jnp.float32) / math.sqrt(span_len)
    return (out * factor).astype(jnp.bfloat16).reshape(2, channels, rows)


def shards(voltages, prototype, input_gain, usable):
    members = voltages.shape[0]
    spectra = channelize(voltages, prototype, input_gain, usable)
    _, channels, rows = spectra.shape
    frames_own = rows // members
    n_inp = lax.axis_size("inp")
    n_wide = lax.axis_size("wide")
    n_dev = n_inp * n_wide
    group_width = channels // n_dev
    chunks = spectra.reshape(2, n_dev, group_width, rows).transpose(1, 0, 2, 3)
    arrived = lax.all_to_all(chunks, ("wide", "inp"), 0, 0, tiled=True)
    arrived = arrived.reshape(n_wide, n_inp, 2, group_width, frames_own, members)
    depth = n_wide * group_width * frames_own
    every = arrived.transpose(2, 0, 3, 4, 1, 5).reshape(2, depth, n_inp * members)
    real_part, imag_part = every[0], every[1]
    left = jnp.stack(
        [jnp.concatenate([real_part, imag_part], axis=0), jnp.concatenate([imag_part, -real_part], axis=0)]
    )
    right = jnp.concatenate([real_part, imag_part], axis=0)
    normalize = 1.0 / math.sqrt(depth)
    left = left.reshape(2, 2 * depth, n_inp, members)
    products = jnp.einsum("pkja,kb->jpab", left, right, preferred_element_type=jnp.float32) * normalize
    spread = lax.all_to_all(products, "inp", 0, 0, tiled=True)
    return spread.transpose(1, 0, 2, 3)


def solution(mesh):
    return jax.shard_map(
        shards,
        mesh=mesh,
        in_specs=(P("inp", "wide"), P(), P("inp"), P("inp")),
        out_specs=P(None, "wide", "inp", None),
        check_vma=False,
    )
```

```python
import math

import jax
import jax.numpy as jnp
from jax import lax
from jax.sharding import PartitionSpec as P

AVG = 16


def passed_along(value, axis, steps):
    count = lax.axis_size(axis)
    initial, last = (max(0, -steps), min(count, count - steps))
    return lax.ppermute(value, axis, [(source, source + steps) for source in range(initial, last)])


def phase_tables(rows_count, cols_count, modulus):
    first_index = jnp.arange(rows_count, dtype=jnp.int32)[:, None]
    second_index = jnp.arange(cols_count, dtype=jnp.int32)[None, :]
    angle = (first_index * second_index % modulus).astype(jnp.float32) * (2.0 * math.pi / modulus)
    return (jnp.cos(angle), jnp.sin(angle))


def filter_frames(voltages, prototype):
    members, width_all = voltages.shape
    taps_count, span_len = prototype.shape
    frames_own = width_all // span_len
    samples = [voltages[:, f * span_len : (f + 1) * span_len].astype(jnp.float32) for f in range(frames_own)]
    near = []
    for f in range(frames_own):
        total = prototype[0][None, :] * samples[f]
        for tap_index in range(1, min(f, taps_count - 1) + 1):
            total = total + prototype[tap_index][None, :] * samples[f - tap_index]
        near.append(total)
    edge_parts = []
    for frame_index in range(taps_count - 1):
        partial_sum = jnp.zeros((members, span_len), jnp.float32)
        for tap_index in range(frame_index + 1, taps_count):
            partial_sum = partial_sum + prototype[tap_index][None, :] * samples[frames_own + frame_index - tap_index]
        edge_parts.append(partial_sum)
    outgoing = jnp.stack(edge_parts).astype(jnp.bfloat16)
    incoming = passed_along(outgoing, "wide", 1).astype(jnp.float32)
    rows = [near[f] + incoming[f] if f < taps_count - 1 else near[f] for f in range(frames_own)]
    return jnp.stack(rows)


def channelize(voltages, prototype, input_gain, usable):
    members = voltages.shape[0]
    span_len = prototype.shape[1]
    channels = span_len // 2
    filtered = filter_frames(voltages, prototype)
    frames_own = filtered.shape[0]
    rows = frames_own * members
    inner_len = min(span_len, 128)
    outer_len = span_len // inner_len
    kept_count = channels // outer_len
    highest = lax.Precision.HIGHEST
    shaped = filtered.reshape(rows, outer_len, inner_len)
    cos_one, sin_one = phase_tables(outer_len, outer_len, outer_len)
    first = jnp.concatenate([cos_one, -sin_one], axis=0)
    stage = jnp.einsum("ka,ran->krn", first, shaped, precision=highest)
    stage_real, stage_imag = stage[:outer_len], stage[outer_len:]
    cos_two, sin_two = phase_tables(outer_len, inner_len, span_len)
    turned_real = stage_real * cos_two[:, None, :] + stage_imag * sin_two[:, None, :]
    turned_imag = stage_imag * cos_two[:, None, :] - stage_real * sin_two[:, None, :]
    turned = jnp.concatenate([turned_real, turned_imag], axis=2)
    cos_three, sin_three = phase_tables(kept_count, inner_len, inner_len)
    second = jnp.concatenate(
        [jnp.concatenate([cos_three, sin_three], axis=1), jnp.concatenate([-sin_three, cos_three], axis=1)], axis=0
    )
    out = jnp.einsum("mn,krn->mkr", second, turned, precision=highest)
    out = out.reshape(2, channels, frames_own, members)
    factor = input_gain * usable.astype(jnp.float32) / math.sqrt(span_len)
    return (out * factor).astype(jnp.bfloat16).reshape(2, channels, rows)


def shards(voltages, prototype, input_gain, usable):
    members = voltages.shape[0]
    spectra = channelize(voltages, prototype, input_gain, usable)
    _, channels, rows = spectra.shape
    frames_own = rows // members
    n_inp = lax.axis_size("inp")
    n_wide = lax.axis_size("wide")
    n_dev = n_inp * n_wide
    group_width = channels // n_dev
    chunks = spectra.reshape(2, n_dev, group_width, rows).transpose(1, 0, 2, 3)
    arrived = lax.all_to_all(chunks, ("wide", "inp"), 0, 0, tiled=True)
    arrived = arrived.reshape(n_wide, n_inp, 2, group_width, frames_own, members)
    depth = n_wide * group_width * frames_own
    every = arrived.transpose(2, 1, 5, 0, 3, 4).reshape(2, n_inp * members, depth)
    real_part, imag_part = every[0], every[1]
    right = jnp.concatenate([real_part, imag_part], axis=1)
    left = jnp.stack([right, jnp.concatenate([imag_part, -real_part], axis=1)])
    normalize = 1.0 / math.sqrt(depth)
    left = left.reshape(2, n_inp, members, left.shape[-1]).transpose(1, 0, 2, 3)
    products = jnp.einsum("jpak,bk->jpab", left, right, preferred_element_type=jnp.float32) * normalize
    spread = lax.all_to_all(products, "inp", 0, 0, tiled=True)
    return spread.transpose(1, 0, 2, 3)


def solution(mesh):
    return jax.shard_map(
        shards,
        mesh=mesh,
        in_specs=(P("inp", "wide"), P(), P("inp"), P("inp")),
        out_specs=P(None, "wide", "inp", None),
        check_vma=False,
    )
```

```python
import math

import jax
import jax.numpy as jnp
from jax import lax
from jax.sharding import PartitionSpec as P

AVG = 16


def passed_along(value, axis, steps):
    count = lax.axis_size(axis)
    initial, last = (max(0, -steps), min(count, count - steps))
    return lax.ppermute(value, axis, [(source, source + steps) for source in range(initial, last)])


def phase_tables(rows_count, cols_count, modulus):
    first_index = jnp.arange(rows_count, dtype=jnp.int32)[:, None]
    second_index = jnp.arange(cols_count, dtype=jnp.int32)[None, :]
    angle = (first_index * second_index % modulus).astype(jnp.float32) * (2.0 * math.pi / modulus)
    return (jnp.cos(angle), jnp.sin(angle))


def filter_frames(voltages, prototype):
    members, width_all = voltages.shape
    taps_count, span_len = prototype.shape
    frames_own = width_all // span_len
    samples = [voltages[:, f * span_len : (f + 1) * span_len].astype(jnp.float32) for f in range(frames_own)]
    near = []
    for f in range(frames_own):
        total = prototype[0][None, :] * samples[f]
        for tap_index in range(1, min(f, taps_count - 1) + 1):
            total = total + prototype[tap_index][None, :] * samples[f - tap_index]
        near.append(total)
    edge_parts = []
    for frame_index in range(taps_count - 1):
        partial_sum = jnp.zeros((members, span_len), jnp.float32)
        for tap_index in range(frame_index + 1, taps_count):
            partial_sum = partial_sum + prototype[tap_index][None, :] * samples[frames_own + frame_index - tap_index]
        edge_parts.append(partial_sum)
    outgoing = jnp.stack(edge_parts).astype(jnp.bfloat16)
    incoming = passed_along(outgoing, "wide", 1).astype(jnp.float32)
    rows = [near[f] + incoming[f] if f < taps_count - 1 else near[f] for f in range(frames_own)]
    return jnp.stack(rows)


def channelize(voltages, prototype, input_gain, usable):
    members = voltages.shape[0]
    span_len = prototype.shape[1]
    channels = span_len // 2
    filtered = filter_frames(voltages, prototype)
    frames_own = filtered.shape[0]
    rows = frames_own * members
    inner_len = min(span_len, 128)
    outer_len = span_len // inner_len
    kept_count = channels // outer_len
    highest = lax.Precision.HIGHEST
    shaped = filtered.reshape(rows, outer_len, inner_len)
    cos_one, sin_one = phase_tables(outer_len, outer_len, outer_len)
    first = jnp.concatenate([cos_one, -sin_one], axis=0)
    stage = jnp.einsum("ka,ran->krn", first, shaped, precision=highest)
    stage_real, stage_imag = stage[:outer_len], stage[outer_len:]
    cos_two, sin_two = phase_tables(outer_len, inner_len, span_len)
    turned_real = stage_real * cos_two[:, None, :] + stage_imag * sin_two[:, None, :]
    turned_imag = stage_imag * cos_two[:, None, :] - stage_real * sin_two[:, None, :]
    turned = jnp.concatenate([turned_real, turned_imag], axis=2)
    cos_three, sin_three = phase_tables(kept_count, inner_len, inner_len)
    second = jnp.concatenate(
        [jnp.concatenate([cos_three, sin_three], axis=1), jnp.concatenate([-sin_three, cos_three], axis=1)], axis=0
    )
    out = jnp.einsum("mn,krn->mkr", second, turned, precision=highest)
    out = out.reshape(2, channels, frames_own, members)
    factor = input_gain * usable.astype(jnp.float32) / math.sqrt(span_len)
    return (out * factor).astype(jnp.bfloat16).reshape(2, channels, rows)


def shards(voltages, prototype, input_gain, usable):
    members = voltages.shape[0]
    spectra = channelize(voltages, prototype, input_gain, usable)
    _, channels, rows = spectra.shape
    frames_own = rows // members
    n_inp = lax.axis_size("inp")
    n_wide = lax.axis_size("wide")
    n_dev = n_inp * n_wide
    group_width = channels // n_dev
    chunks = spectra.reshape(2, n_dev, group_width, rows).transpose(1, 0, 2, 3)
    lane = 128
    flat = chunks.reshape(n_dev, (2 * group_width * rows) // lane, lane)
    arrived = lax.all_to_all(flat, ("wide", "inp"), 0, 0, tiled=True)
    arrived = arrived.reshape(n_wide, n_inp, 2, group_width, frames_own, members)
    depth = n_wide * group_width * frames_own
    both = arrived.transpose(1, 5, 2, 0, 3, 4).reshape(n_inp * members, 2 * depth)
    turned = jnp.concatenate([both[:, depth:], -both[:, :depth]], axis=1)
    normalize = 1.0 / math.sqrt(depth)
    left = jnp.stack([both.reshape(n_inp, members, 2 * depth), turned.reshape(n_inp, members, 2 * depth)], axis=1)
    products = jnp.einsum("jpak,bk->jpab", left, both, preferred_element_type=jnp.float32) * normalize
    spread = lax.all_to_all(products, "inp", 0, 0, tiled=True)
    return spread.transpose(1, 0, 2, 3)


def solution(mesh):
    return jax.shard_map(
        shards,
        mesh=mesh,
        in_specs=(P("inp", "wide"), P(), P("inp"), P("inp")),
        out_specs=P(None, "wide", "inp", None),
        check_vma=False,
    )
```

```python
import math

import jax
import jax.numpy as jnp
from jax import lax
from jax.sharding import PartitionSpec as P

AVG = 16


def passed_along(value, axis, steps):
    count = lax.axis_size(axis)
    initial, last = (max(0, -steps), min(count, count - steps))
    return lax.ppermute(value, axis, [(source, source + steps) for source in range(initial, last)])


def phase_tables(rows_count, cols_count, modulus):
    first_index = jnp.arange(rows_count, dtype=jnp.int32)[:, None]
    second_index = jnp.arange(cols_count, dtype=jnp.int32)[None, :]
    angle = (first_index * second_index % modulus).astype(jnp.float32) * (2.0 * math.pi / modulus)
    return (jnp.cos(angle), jnp.sin(angle))


def filter_frames(voltages, prototype):
    members, width_all = voltages.shape
    taps_count, span_len = prototype.shape
    frames_own = width_all // span_len
    samples = [voltages[:, f * span_len : (f + 1) * span_len].astype(jnp.float32) for f in range(frames_own)]
    near = []
    for f in range(frames_own):
        total = prototype[0][None, :] * samples[f]
        for tap_index in range(1, min(f, taps_count - 1) + 1):
            total = total + prototype[tap_index][None, :] * samples[f - tap_index]
        near.append(total)
    edge_parts = []
    for frame_index in range(taps_count - 1):
        partial_sum = jnp.zeros((members, span_len), jnp.float32)
        for tap_index in range(frame_index + 1, taps_count):
            partial_sum = partial_sum + prototype[tap_index][None, :] * samples[frames_own + frame_index - tap_index]
        edge_parts.append(partial_sum)
    outgoing = jnp.stack(edge_parts).astype(jnp.bfloat16)
    incoming = passed_along(outgoing, "wide", 1).astype(jnp.float32)
    rows = [near[f] + incoming[f] if f < taps_count - 1 else near[f] for f in range(frames_own)]
    return jnp.stack(rows)


def channelize(voltages, prototype, input_gain, usable):
    members = voltages.shape[0]
    span_len = prototype.shape[1]
    channels = span_len // 2
    filtered = filter_frames(voltages, prototype)
    frames_own = filtered.shape[0]
    rows = frames_own * members
    inner_len = min(span_len, 128)
    outer_len = span_len // inner_len
    kept_count = channels // outer_len
    highest = lax.Precision.HIGHEST
    shaped = filtered.reshape(rows, outer_len, inner_len)
    cos_one, sin_one = phase_tables(outer_len, outer_len, outer_len)
    first = jnp.concatenate([cos_one, -sin_one], axis=0)
    stage = jnp.einsum("ka,ran->krn", first, shaped, precision=highest)
    stage_real, stage_imag = stage[:outer_len], stage[outer_len:]
    cos_two, sin_two = phase_tables(outer_len, inner_len, span_len)
    turned_real = stage_real * cos_two[:, None, :] + stage_imag * sin_two[:, None, :]
    turned_imag = stage_imag * cos_two[:, None, :] - stage_real * sin_two[:, None, :]
    turned = jnp.stack([turned_real, turned_imag])
    cos_three, sin_three = phase_tables(kept_count, inner_len, inner_len)
    second = jnp.stack(
        [jnp.stack([cos_three, sin_three], axis=1), jnp.stack([-sin_three, cos_three], axis=1)]
    )
    out = jnp.einsum("pmqn,qkrn->pmkr", second, turned, precision=highest)
    out = out.reshape(2, channels, frames_own, members)
    factor = input_gain * usable.astype(jnp.float32) / math.sqrt(span_len)
    return (out * factor).astype(jnp.bfloat16).reshape(2, channels, rows)


def shards(voltages, prototype, input_gain, usable):
    members = voltages.shape[0]
    spectra = channelize(voltages, prototype, input_gain, usable)
    _, channels, rows = spectra.shape
    frames_own = rows // members
    n_inp = lax.axis_size("inp")
    n_wide = lax.axis_size("wide")
    n_dev = n_inp * n_wide
    group_width = channels // n_dev
    chunks = spectra.reshape(2, n_dev, group_width, rows).transpose(1, 0, 2, 3)
    arrived = lax.all_to_all(chunks, ("wide", "inp"), 0, 0, tiled=True)
    arrived = arrived.reshape(n_wide, n_inp, 2, group_width, frames_own, members)
    depth = n_wide * group_width * frames_own
    every = arrived.transpose(2, 1, 5, 0, 3, 4).reshape(2, n_inp * members, depth)
    real_part, imag_part = every[0], every[1]
    right = jnp.concatenate([real_part, imag_part], axis=1)
    left = jnp.stack([right, jnp.concatenate([imag_part, -real_part], axis=1)])
    normalize = 1.0 / math.sqrt(depth)
    left = left.reshape(2, n_inp, members, left.shape[-1]).transpose(1, 0, 2, 3)
    products = jnp.einsum("jpak,bk->jpab", left, right, preferred_element_type=jnp.float32) * normalize
    spread = lax.all_to_all(products, "inp", 0, 0, tiled=True)
    return spread.transpose(1, 0, 2, 3)


def solution(mesh):
    return jax.shard_map(
        shards,
        mesh=mesh,
        in_specs=(P("inp", "wide"), P(), P("inp"), P("inp")),
        out_specs=P(None, "wide", "inp", None),
        check_vma=False,
    )
```

```python
import math

import jax
import jax.numpy as jnp
from jax import lax
from jax.sharding import PartitionSpec as P

AVG = 16


def passed_along(value, axis, steps):
    count = lax.axis_size(axis)
    initial, last = (max(0, -steps), min(count, count - steps))
    return lax.ppermute(value, axis, [(source, source + steps) for source in range(initial, last)])


def phase_tables(rows_count, cols_count, modulus):
    first_index = jnp.arange(rows_count, dtype=jnp.int32)[:, None]
    second_index = jnp.arange(cols_count, dtype=jnp.int32)[None, :]
    angle = (first_index * second_index % modulus).astype(jnp.float32) * (2.0 * math.pi / modulus)
    return (jnp.cos(angle), jnp.sin(angle))


def filter_frames(voltages, prototype):
    members, width_all = voltages.shape
    taps_count, span_len = prototype.shape
    frames_own = width_all // span_len
    samples = [voltages[:, f * span_len : (f + 1) * span_len].astype(jnp.float32) for f in range(frames_own)]
    near = []
    for f in range(frames_own):
        total = prototype[0][None, :] * samples[f]
        for tap_index in range(1, min(f, taps_count - 1) + 1):
            total = total + prototype[tap_index][None, :] * samples[f - tap_index]
        near.append(total)
    edge_parts = []
    for frame_index in range(taps_count - 1):
        partial_sum = jnp.zeros((members, span_len), jnp.float32)
        for tap_index in range(frame_index + 1, taps_count):
            partial_sum = partial_sum + prototype[tap_index][None, :] * samples[frames_own + frame_index - tap_index]
        edge_parts.append(partial_sum)
    outgoing = jnp.stack(edge_parts).astype(jnp.bfloat16)
    incoming = passed_along(outgoing, "wide", 1).astype(jnp.float32)
    rows = [near[f] + incoming[f] if f < taps_count - 1 else near[f] for f in range(frames_own)]
    return jnp.stack(rows)


def channelize(voltages, prototype, input_gain, usable):
    members = voltages.shape[0]
    span_len = prototype.shape[1]
    channels = span_len // 2
    filtered = filter_frames(voltages, prototype)
    frames_own = filtered.shape[0]
    rows = frames_own * members
    inner_len = min(span_len, 128)
    outer_len = span_len // inner_len
    kept_count = channels // outer_len
    precise = lax.Precision.HIGH
    shaped = filtered.reshape(rows, outer_len, inner_len)
    cos_one, sin_one = phase_tables(outer_len, outer_len, outer_len)
    first = jnp.stack([cos_one, -sin_one])
    stage = jnp.einsum("qka,ran->qkrn", first, shaped, precision=precise)
    cos_two, sin_two = phase_tables(outer_len, inner_len, span_len)
    signs = jnp.array([1.0, -1.0], jnp.float32)[:, None, None, None]
    turned = stage * cos_two[None, :, None, :] + stage[::-1] * (signs * sin_two[None, :, None, :])
    cos_three, sin_three = phase_tables(kept_count, inner_len, inner_len)
    second = jnp.stack(
        [jnp.stack([cos_three, sin_three], axis=1), jnp.stack([-sin_three, cos_three], axis=1)]
    )
    out = jnp.einsum("pmqn,qkrn->pmkr", second, turned, precision=precise)
    out = out.reshape(2, channels, frames_own, members)
    factor = input_gain * usable.astype(jnp.float32) / math.sqrt(span_len)
    return (out * factor).astype(jnp.bfloat16).reshape(2, channels, rows)


def shards(voltages, prototype, input_gain, usable):
    members = voltages.shape[0]
    spectra = channelize(voltages, prototype, input_gain, usable)
    _, channels, rows = spectra.shape
    frames_own = rows // members
    n_inp = lax.axis_size("inp")
    n_wide = lax.axis_size("wide")
    n_dev = n_inp * n_wide
    group_width = channels // n_dev
    chunks = spectra.reshape(2, n_dev, group_width, rows).transpose(1, 0, 2, 3)
    arrived = lax.all_to_all(chunks, ("wide", "inp"), 0, 0, tiled=True)
    arrived = arrived.reshape(n_wide, n_inp, 2, group_width, frames_own, members)
    depth = n_wide * group_width * frames_own
    every = arrived.transpose(2, 1, 5, 0, 3, 4).reshape(2, n_inp * members, depth)
    real_part, imag_part = every[0], every[1]
    right = jnp.concatenate([real_part, imag_part], axis=1)
    left = jnp.stack([right, jnp.concatenate([imag_part, -real_part], axis=1)])
    normalize = 1.0 / math.sqrt(depth)
    left = left.reshape(2, n_inp, members, left.shape[-1]).transpose(1, 0, 2, 3)
    products = jnp.einsum("jpak,bk->jpab", left, right, preferred_element_type=jnp.float32) * normalize
    spread = lax.all_to_all(products, "inp", 0, 0, tiled=True)
    return spread.transpose(1, 0, 2, 3)


def solution(mesh):
    return jax.shard_map(
        shards,
        mesh=mesh,
        in_specs=(P("inp", "wide"), P(), P("inp"), P("inp")),
        out_specs=P(None, "wide", "inp", None),
        check_vma=False,
    )
```

```python
import math

import jax
import jax.numpy as jnp
from jax import lax
from jax.sharding import PartitionSpec as P

AVG = 16


def passed_along(value, axis, steps):
    count = lax.axis_size(axis)
    initial, last = (max(0, -steps), min(count, count - steps))
    return lax.ppermute(value, axis, [(source, source + steps) for source in range(initial, last)])


def phase_tables(rows_count, cols_count, modulus):
    first_index = jnp.arange(rows_count, dtype=jnp.int32)[:, None]
    second_index = jnp.arange(cols_count, dtype=jnp.int32)[None, :]
    angle = (first_index * second_index % modulus).astype(jnp.float32) * (2.0 * math.pi / modulus)
    return (jnp.cos(angle), jnp.sin(angle))


def filter_frames(voltages, prototype):
    members, width_all = voltages.shape
    taps_count, span_len = prototype.shape
    frames_own = width_all // span_len
    samples = [voltages[:, f * span_len : (f + 1) * span_len].astype(jnp.float32) for f in range(frames_own)]
    near = []
    for f in range(frames_own):
        total = prototype[0][None, :] * samples[f]
        for tap_index in range(1, min(f, taps_count - 1) + 1):
            total = total + prototype[tap_index][None, :] * samples[f - tap_index]
        near.append(total)
    rows = []
    for f in range(frames_own):
        if f >= taps_count - 1:
            rows.append((near[f], None))
            continue
        partial_sum = jnp.zeros((members, span_len), jnp.float32)
        for tap_index in range(f + 1, taps_count):
            partial_sum = partial_sum + prototype[tap_index][None, :] * samples[frames_own + f - tap_index]
        rows.append((near[f], passed_along(partial_sum.astype(jnp.bfloat16), "wide", 1)))
    return rows


def transform_rows(filtered, channels):
    rows, span_len = filtered.shape
    inner_len = min(span_len, 128)
    outer_len = span_len // inner_len
    kept_count = channels // outer_len
    precise = lax.Precision.HIGH
    shaped = filtered.reshape(rows, outer_len, inner_len)
    cos_one, sin_one = phase_tables(outer_len, outer_len, outer_len)
    first = jnp.stack([cos_one, -sin_one])
    stage = jnp.einsum("qka,ran->qkrn", first, shaped, precision=precise)
    cos_two, sin_two = phase_tables(outer_len, inner_len, span_len)
    signs = jnp.array([1.0, -1.0], jnp.float32)[:, None, None, None]
    turned = stage * cos_two[None, :, None, :] + stage[::-1] * (signs * sin_two[None, :, None, :])
    cos_three, sin_three = phase_tables(kept_count, inner_len, inner_len)
    second = jnp.stack(
        [jnp.stack([cos_three, sin_three], axis=1), jnp.stack([-sin_three, cos_three], axis=1)]
    )
    out = jnp.einsum("pmqn,qkrn->pmkr", second, turned, precision=precise)
    return out.reshape(2, channels, rows)


def channelize(voltages, prototype, input_gain, usable):
    members = voltages.shape[0]
    span_len = prototype.shape[1]
    channels = span_len // 2
    filtered = filter_frames(voltages, prototype)
    outs = []
    for near, incoming in filtered:
        if incoming is not None:
            if outs:
                outs[-1], incoming = lax.optimization_barrier((outs[-1], incoming))
            near = near + incoming.astype(jnp.float32)
        outs.append(transform_rows(near, channels))
    out = jnp.stack(outs, axis=2)
    factor = input_gain * usable.astype(jnp.float32) / math.sqrt(span_len)
    return (out * factor).astype(jnp.bfloat16).reshape(2, channels, len(filtered) * members)


def shards(voltages, prototype, input_gain, usable):
    members = voltages.shape[0]
    spectra = channelize(voltages, prototype, input_gain, usable)
    _, channels, rows = spectra.shape
    frames_own = rows // members
    n_inp = lax.axis_size("inp")
    n_wide = lax.axis_size("wide")
    n_dev = n_inp * n_wide
    group_width = channels // n_dev
    chunks = spectra.reshape(2, n_dev, group_width, rows).transpose(1, 0, 2, 3)
    arrived = lax.all_to_all(chunks, ("wide", "inp"), 0, 0, tiled=True)
    arrived = arrived.reshape(n_wide, n_inp, 2, group_width, frames_own, members)
    depth = n_wide * group_width * frames_own
    every = arrived.transpose(2, 1, 5, 0, 3, 4).reshape(2, n_inp * members, depth)
    real_part, imag_part = every[0], every[1]
    right = jnp.concatenate([real_part, imag_part], axis=1)
    left = jnp.stack([right, jnp.concatenate([imag_part, -real_part], axis=1)])
    normalize = 1.0 / math.sqrt(depth)
    left = left.reshape(2, n_inp, members, left.shape[-1]).transpose(1, 0, 2, 3)
    products = jnp.einsum("jpak,bk->jpab", left, right, preferred_element_type=jnp.float32) * normalize
    spread = lax.all_to_all(products, "inp", 0, 0, tiled=True)
    return spread.transpose(1, 0, 2, 3)


def solution(mesh):
    return jax.shard_map(
        shards,
        mesh=mesh,
        in_specs=(P("inp", "wide"), P(), P("inp"), P("inp")),
        out_specs=P(None, "wide", "inp", None),
        check_vma=False,
    )
```

```python
import math

import jax
import jax.numpy as jnp
from jax import lax
from jax.sharding import PartitionSpec as P

AVG = 16


def passed_along(value, axis, steps):
    count = lax.axis_size(axis)
    initial, last = (max(0, -steps), min(count, count - steps))
    return lax.ppermute(value, axis, [(source, source + steps) for source in range(initial, last)])


def phase_tables(rows_count, cols_count, modulus):
    first_index = jnp.arange(rows_count, dtype=jnp.int32)[:, None]
    second_index = jnp.arange(cols_count, dtype=jnp.int32)[None, :]
    angle = (first_index * second_index % modulus).astype(jnp.float32) * (2.0 * math.pi / modulus)
    return (jnp.cos(angle), jnp.sin(angle))


def filter_frames(voltages, prototype):
    members, width_all = voltages.shape
    taps_count, span_len = prototype.shape
    frames_own = width_all // span_len
    samples = [voltages[:, f * span_len : (f + 1) * span_len].astype(jnp.float32) for f in range(frames_own)]
    near = []
    for f in range(frames_own):
        total = prototype[0][None, :] * samples[f]
        for tap_index in range(1, min(f, taps_count - 1) + 1):
            total = total + prototype[tap_index][None, :] * samples[f - tap_index]
        near.append(total)
    rows = []
    for f in range(frames_own):
        if f >= taps_count - 1:
            rows.append((near[f], None))
            continue
        partial_sum = jnp.zeros((members, span_len), jnp.float32)
        for tap_index in range(f + 1, taps_count):
            partial_sum = partial_sum + prototype[tap_index][None, :] * samples[frames_own + f - tap_index]
        rows.append((near[f], passed_along(partial_sum.astype(jnp.bfloat16), "wide", 1)))
    return rows


def transform_rows(filtered, channels):
    rows, span_len = filtered.shape
    inner_len = min(span_len, 128)
    outer_len = span_len // inner_len
    kept_count = channels // outer_len
    precise = lax.Precision.HIGH
    shaped = filtered.reshape(rows, outer_len, inner_len)
    cos_one, sin_one = phase_tables(outer_len, outer_len, outer_len)
    first = jnp.stack([cos_one, -sin_one])
    stage = jnp.einsum("qka,ran->qkrn", first, shaped, precision=precise)
    cos_two, sin_two = phase_tables(outer_len, inner_len, span_len)
    signs = jnp.array([1.0, -1.0], jnp.float32)[:, None, None, None]
    turned = stage * cos_two[None, :, None, :] + stage[::-1] * (signs * sin_two[None, :, None, :])
    cos_three, sin_three = phase_tables(kept_count, inner_len, inner_len)
    second = jnp.stack(
        [jnp.stack([cos_three, sin_three], axis=1), jnp.stack([-sin_three, cos_three], axis=1)]
    )
    out = jnp.einsum("pmqn,qkrn->pmkr", second, turned, precision=precise)
    return out.reshape(2, channels, rows)


def channelize(voltages, prototype, input_gain, usable):
    members = voltages.shape[0]
    span_len = prototype.shape[1]
    channels = span_len // 2
    filtered = filter_frames(voltages, prototype)
    outs = []
    for near, incoming in filtered:
        if incoming is not None:
            if outs:
                outs[-1], incoming = lax.optimization_barrier((outs[-1], incoming))
            near = near + incoming.astype(jnp.float32)
        outs.append(transform_rows(near, channels))
    factor = input_gain * usable.astype(jnp.float32) / math.sqrt(span_len)
    out = jnp.stack([(one * factor).astype(jnp.bfloat16) for one in outs], axis=2)
    return out.reshape(2, channels, len(filtered) * members)


def shards(voltages, prototype, input_gain, usable):
    members = voltages.shape[0]
    spectra = channelize(voltages, prototype, input_gain, usable)
    _, channels, rows = spectra.shape
    frames_own = rows // members
    n_inp = lax.axis_size("inp")
    n_wide = lax.axis_size("wide")
    n_dev = n_inp * n_wide
    group_width = channels // n_dev
    chunks = spectra.reshape(2, n_dev, group_width, rows).transpose(1, 0, 2, 3)
    arrived = lax.all_to_all(chunks, ("wide", "inp"), 0, 0, tiled=True)
    arrived = arrived.reshape(n_wide, n_inp, 2, group_width, frames_own, members)
    depth = n_wide * group_width * frames_own
    every = arrived.transpose(2, 1, 5, 0, 3, 4).reshape(2, n_inp * members, depth)
    real_part, imag_part = every[0], every[1]
    right = jnp.concatenate([real_part, imag_part], axis=1)
    left = jnp.stack([right, jnp.concatenate([imag_part, -real_part], axis=1)])
    normalize = 1.0 / math.sqrt(depth)
    left = left.reshape(2, n_inp, members, left.shape[-1]).transpose(1, 0, 2, 3)
    products = jnp.einsum("jpak,bk->jpab", left, right, preferred_element_type=jnp.float32) * normalize
    spread = lax.all_to_all(products, "inp", 0, 0, tiled=True)
    return spread.transpose(1, 0, 2, 3)


def solution(mesh):
    return jax.shard_map(
        shards,
        mesh=mesh,
        in_specs=(P("inp", "wide"), P(), P("inp"), P("inp")),
        out_specs=P(None, "wide", "inp", None),
        check_vma=False,
    )
```

```python
import math

import jax
import jax.numpy as jnp
from jax import lax
from jax.sharding import PartitionSpec as P

AVG = 16


def passed_along(value, axis, steps):
    count = lax.axis_size(axis)
    initial, last = (max(0, -steps), min(count, count - steps))
    return lax.ppermute(value, axis, [(source, source + steps) for source in range(initial, last)])


def phase_tables(rows_count, cols_count, modulus):
    first_index = jnp.arange(rows_count, dtype=jnp.int32)[:, None]
    second_index = jnp.arange(cols_count, dtype=jnp.int32)[None, :]
    angle = (first_index * second_index % modulus).astype(jnp.float32) * (2.0 * math.pi / modulus)
    return (jnp.cos(angle), jnp.sin(angle))


def filter_frames(voltages, prototype):
    members, width_all = voltages.shape
    taps_count, span_len = prototype.shape
    frames_own = width_all // span_len
    samples = [voltages[:, f * span_len : (f + 1) * span_len].astype(jnp.float32) for f in range(frames_own)]
    near = []
    for f in range(frames_own):
        total = prototype[0][None, :] * samples[f]
        for tap_index in range(1, min(f, taps_count - 1) + 1):
            total = total + prototype[tap_index][None, :] * samples[f - tap_index]
        near.append(total)
    rows = []
    for f in range(frames_own):
        if f >= taps_count - 1:
            rows.append((near[f], None))
            continue
        partial_sum = jnp.zeros((members, span_len), jnp.float32)
        for tap_index in range(f + 1, taps_count):
            partial_sum = partial_sum + prototype[tap_index][None, :] * samples[frames_own + f - tap_index]
        rows.append((near[f], passed_along(partial_sum.astype(jnp.bfloat16), "wide", 1)))
    return rows


def transform_rows(filtered, channels):
    rows, span_len = filtered.shape
    inner_len = min(span_len, 128)
    outer_len = span_len // inner_len
    kept_count = channels // outer_len
    precise = lax.Precision.HIGH
    shaped = filtered.reshape(rows, outer_len, inner_len)
    cos_one, sin_one = phase_tables(outer_len, outer_len, outer_len)
    first = jnp.stack([cos_one, -sin_one])
    stage = jnp.einsum("qka,ran->qkrn", first, shaped, precision=precise)
    cos_two, sin_two = phase_tables(outer_len, inner_len, span_len)
    signs = jnp.array([1.0, -1.0], jnp.float32)[:, None, None, None]
    turned = stage * cos_two[None, :, None, :] + stage[::-1] * (signs * sin_two[None, :, None, :])
    cos_three, sin_three = phase_tables(kept_count, inner_len, inner_len)
    second = jnp.stack(
        [jnp.stack([cos_three, sin_three], axis=1), jnp.stack([-sin_three, cos_three], axis=1)]
    )
    out = jnp.einsum("pmqn,qkrn->pmkr", second, turned, precision=precise)
    return out.reshape(2, channels, rows)


def channelize(voltages, prototype, input_gain, usable):
    members = voltages.shape[0]
    span_len = prototype.shape[1]
    channels = span_len // 2
    filtered = filter_frames(voltages, prototype)
    outs = []
    for near, incoming in filtered:
        if incoming is not None:
            if outs:
                outs[-1], incoming = lax.optimization_barrier((outs[-1], incoming))
            near = near + incoming.astype(jnp.float32)
        outs.append(transform_rows(near, channels))
    factor = input_gain * usable.astype(jnp.float32) / math.sqrt(span_len)
    return jnp.concatenate([(one * factor).astype(jnp.bfloat16) for one in outs], axis=2)


def shards(voltages, prototype, input_gain, usable):
    members = voltages.shape[0]
    spectra = channelize(voltages, prototype, input_gain, usable)
    _, channels, rows = spectra.shape
    frames_own = rows // members
    n_inp = lax.axis_size("inp")
    n_wide = lax.axis_size("wide")
    n_dev = n_inp * n_wide
    group_width = channels // n_dev
    chunks = spectra.reshape(2, n_dev, group_width, rows).transpose(1, 0, 2, 3)
    arrived = lax.all_to_all(chunks, ("wide", "inp"), 0, 0, tiled=True)
    arrived = arrived.reshape(n_wide, n_inp, 2, group_width, frames_own, members)
    depth = n_wide * group_width * frames_own
    every = arrived.transpose(2, 1, 5, 0, 3, 4).reshape(2, n_inp * members, depth)
    real_part, imag_part = every[0], every[1]
    right = jnp.concatenate([real_part, imag_part], axis=1)
    left = jnp.stack([right, jnp.concatenate([imag_part, -real_part], axis=1)])
    normalize = 1.0 / math.sqrt(depth)
    left = left.reshape(2, n_inp, members, left.shape[-1]).transpose(1, 0, 2, 3)
    products = jnp.einsum("jpak,bk->jpab", left, right, preferred_element_type=jnp.float32) * normalize
    spread = lax.all_to_all(products, "inp", 0, 0, tiled=True)
    return spread.transpose(1, 0, 2, 3)


def solution(mesh):
    return jax.shard_map(
        shards,
        mesh=mesh,
        in_specs=(P("inp", "wide"), P(), P("inp"), P("inp")),
        out_specs=P(None, "wide", "inp", None),
        check_vma=False,
    )
```

```python
import math

import jax
import jax.numpy as jnp
from jax import lax
from jax.sharding import PartitionSpec as P

AVG = 16


def passed_along(value, axis, steps):
    count = lax.axis_size(axis)
    initial, last = (max(0, -steps), min(count, count - steps))
    return lax.ppermute(value, axis, [(source, source + steps) for source in range(initial, last)])


def phase_tables(rows_count, cols_count, modulus):
    first_index = jnp.arange(rows_count, dtype=jnp.int32)[:, None]
    second_index = jnp.arange(cols_count, dtype=jnp.int32)[None, :]
    angle = (first_index * second_index % modulus).astype(jnp.float32) * (2.0 * math.pi / modulus)
    return (jnp.cos(angle), jnp.sin(angle))


def filter_frames(voltages, prototype):
    members, width_all = voltages.shape
    taps_count, span_len = prototype.shape
    frames_own = width_all // span_len
    samples = [voltages[:, f * span_len : (f + 1) * span_len].astype(jnp.float32) for f in range(frames_own)]
    near = []
    for f in range(frames_own):
        total = prototype[0][None, :] * samples[f]
        for tap_index in range(1, min(f, taps_count - 1) + 1):
            total = total + prototype[tap_index][None, :] * samples[f - tap_index]
        near.append(total)
    rows = []
    for f in range(frames_own):
        if f >= taps_count - 1:
            rows.append((near[f], None))
            continue
        partial_sum = jnp.zeros((members, span_len), jnp.float32)
        for tap_index in range(f + 1, taps_count):
            partial_sum = partial_sum + prototype[tap_index][None, :] * samples[frames_own + f - tap_index]
        rows.append((near[f], passed_along(partial_sum.astype(jnp.bfloat16), "wide", 1)))
    return rows


def transform_rows(filtered, channels):
    rows, span_len = filtered.shape
    inner_len = min(span_len, 128)
    outer_len = span_len // inner_len
    kept_count = channels // outer_len
    precise = lax.Precision.HIGH
    shaped = filtered.reshape(rows, outer_len, inner_len)
    cos_one, sin_one = phase_tables(outer_len, outer_len, outer_len)
    first = jnp.stack([cos_one, -sin_one])
    stage = jnp.einsum("qka,ran->qkrn", first, shaped, precision=precise)
    cos_two, sin_two = phase_tables(outer_len, inner_len, span_len)
    signs = jnp.array([1.0, -1.0], jnp.float32)[:, None, None, None]
    turned = stage * cos_two[None, :, None, :] + stage[::-1] * (signs * sin_two[None, :, None, :])
    cos_three, sin_three = phase_tables(kept_count, inner_len, inner_len)
    second = jnp.stack(
        [jnp.stack([cos_three, sin_three], axis=1), jnp.stack([-sin_three, cos_three], axis=1)]
    )
    out = jnp.einsum("pmqn,qkrn->pmkr", second, turned, precision=precise)
    return out.reshape(2, channels, rows)


def channelize(voltages, prototype, input_gain, usable):
    members = voltages.shape[0]
    span_len = prototype.shape[1]
    channels = span_len // 2
    filtered = filter_frames(voltages, prototype)
    outs = []
    for near, incoming in filtered:
        if incoming is not None:
            if outs:
                outs[-1], incoming = lax.optimization_barrier((outs[-1], incoming))
            near = near + incoming.astype(jnp.float32)
        outs.append(transform_rows(near, channels))
    factor = input_gain * usable.astype(jnp.float32) / math.sqrt(span_len)
    return jnp.concatenate([(one * factor).astype(jnp.bfloat16) for one in outs], axis=2)


def shards(voltages, prototype, input_gain, usable):
    members = voltages.shape[0]
    spectra = channelize(voltages, prototype, input_gain, usable)
    _, channels, rows = spectra.shape
    frames_own = rows // members
    n_inp = lax.axis_size("inp")
    n_wide = lax.axis_size("wide")
    n_dev = n_inp * n_wide
    group_width = channels // n_dev
    chunks = spectra.reshape(2, n_dev, group_width, rows).transpose(1, 0, 2, 3)
    arrived = lax.all_to_all(chunks, ("wide", "inp"), 0, 0, tiled=True)
    arrived = arrived.reshape(n_wide, n_inp, 2, group_width, rows)
    depth = n_wide * group_width * frames_own
    real_part, imag_part = (
        jnp.concatenate(
            [
                arrived[:, :, part, :, f * members : (f + 1) * members]
                .transpose(1, 3, 0, 2)
                .reshape(n_inp * members, n_wide * group_width)
                for f in range(frames_own)
            ],
            axis=1,
        )
        for part in range(2)
    )
    right = jnp.concatenate([real_part, imag_part], axis=1)
    left = jnp.stack([right, jnp.concatenate([imag_part, -real_part], axis=1)])
    normalize = 1.0 / math.sqrt(depth)
    left = left.reshape(2, n_inp, members, left.shape[-1]).transpose(1, 0, 2, 3)
    products = jnp.einsum("jpak,bk->jpab", left, right, preferred_element_type=jnp.float32) * normalize
    spread = lax.all_to_all(products, "inp", 0, 0, tiled=True)
    return spread.transpose(1, 0, 2, 3)


def solution(mesh):
    return jax.shard_map(
        shards,
        mesh=mesh,
        in_specs=(P("inp", "wide"), P(), P("inp"), P("inp")),
        out_specs=P(None, "wide", "inp", None),
        check_vma=False,
    )
```

```python
import math

import jax
import jax.numpy as jnp
from jax import lax
from jax.sharding import PartitionSpec as P

AVG = 16


def passed_along(value, axis, steps):
    count = lax.axis_size(axis)
    initial, last = (max(0, -steps), min(count, count - steps))
    return lax.ppermute(value, axis, [(source, source + steps) for source in range(initial, last)])


def phase_tables(rows_count, cols_count, modulus):
    first_index = jnp.arange(rows_count, dtype=jnp.int32)[:, None]
    second_index = jnp.arange(cols_count, dtype=jnp.int32)[None, :]
    angle = (first_index * second_index % modulus).astype(jnp.float32) * (2.0 * math.pi / modulus)
    return (jnp.cos(angle), jnp.sin(angle))


def filter_frames(voltages, prototype):
    members, width_all = voltages.shape
    taps_count, span_len = prototype.shape
    frames_own = width_all // span_len
    samples = [voltages[:, f * span_len : (f + 1) * span_len].astype(jnp.float32) for f in range(frames_own)]
    near = []
    for f in range(frames_own):
        total = prototype[0][None, :] * samples[f]
        for tap_index in range(1, min(f, taps_count - 1) + 1):
            total = total + prototype[tap_index][None, :] * samples[f - tap_index]
        near.append(total)
    rows = []
    for f in range(frames_own):
        if f >= taps_count - 1:
            rows.append((near[f], None))
            continue
        partial_sum = jnp.zeros((members, span_len), jnp.float32)
        for tap_index in range(f + 1, taps_count):
            partial_sum = partial_sum + prototype[tap_index][None, :] * samples[frames_own + f - tap_index]
        rows.append((near[f], passed_along(partial_sum.astype(jnp.bfloat16), "wide", 1)))
    return rows


def transform_rows(filtered, channels):
    rows, span_len = filtered.shape
    inner_len = min(span_len, 128)
    outer_len = span_len // inner_len
    kept_count = channels // outer_len
    precise = lax.Precision.HIGH
    shaped = filtered.reshape(rows, outer_len, inner_len)
    cos_one, sin_one = phase_tables(outer_len, outer_len, outer_len)
    first = jnp.stack([cos_one, -sin_one])
    stage = jnp.einsum("qka,ran->qkrn", first, shaped, precision=precise)
    cos_two, sin_two = phase_tables(outer_len, inner_len, span_len)
    signs = jnp.array([1.0, -1.0], jnp.float32)[:, None, None, None]
    turned = stage * cos_two[None, :, None, :] + stage[::-1] * (signs * sin_two[None, :, None, :])
    cos_three, sin_three = phase_tables(kept_count, inner_len, inner_len)
    second = jnp.stack(
        [jnp.stack([cos_three, sin_three], axis=1), jnp.stack([-sin_three, cos_three], axis=1)]
    )
    out = jnp.einsum("pmqn,qkrn->pmkr", second, turned, precision=precise)
    return out.reshape(2, channels, rows)


def channelize(voltages, prototype, input_gain, usable):
    members = voltages.shape[0]
    span_len = prototype.shape[1]
    channels = span_len // 2
    filtered = filter_frames(voltages, prototype)
    outs = []
    for near, incoming in filtered:
        if incoming is not None:
            if outs:
                outs[-1], incoming = lax.optimization_barrier((outs[-1], incoming))
            near = near + incoming.astype(jnp.float32)
        outs.append(transform_rows(near, channels))
    factor = input_gain * usable.astype(jnp.float32) / math.sqrt(span_len)
    return jnp.concatenate([(one * factor).astype(jnp.bfloat16) for one in outs], axis=2)


def shards(voltages, prototype, input_gain, usable):
    members = voltages.shape[0]
    spectra = channelize(voltages, prototype, input_gain, usable)
    _, channels, rows = spectra.shape
    frames_own = rows // members
    n_inp = lax.axis_size("inp")
    n_wide = lax.axis_size("wide")
    n_dev = n_inp * n_wide
    group_width = channels // n_dev
    chunks = spectra.reshape(2, n_wide, n_inp, group_width, rows).transpose(2, 1, 0, 3, 4)
    chunks = chunks.reshape(n_dev, 2, group_width, rows)
    arrived = lax.all_to_all(chunks, ("inp", "wide"), 0, 0, tiled=True)
    arrived = arrived.reshape(n_inp, n_wide, 2, group_width, rows)
    depth = n_wide * group_width * frames_own
    real_part, imag_part = (
        jnp.concatenate(
            [
                arrived[:, :, part, :, f * members : (f + 1) * members]
                .transpose(0, 3, 1, 2)
                .reshape(n_inp * members, n_wide * group_width)
                for f in range(frames_own)
            ],
            axis=1,
        )
        for part in range(2)
    )
    right = jnp.concatenate([real_part, imag_part], axis=1)
    left = jnp.stack([right, jnp.concatenate([imag_part, -real_part], axis=1)])
    normalize = 1.0 / math.sqrt(depth)
    left = left.reshape(2, n_inp, members, left.shape[-1]).transpose(1, 0, 2, 3)
    products = jnp.einsum("jpak,bk->jpab", left, right, preferred_element_type=jnp.float32) * normalize
    spread = lax.all_to_all(products, "inp", 0, 0, tiled=True)
    return spread.transpose(1, 0, 2, 3)


def solution(mesh):
    return jax.shard_map(
        shards,
        mesh=mesh,
        in_specs=(P("inp", "wide"), P(), P("inp"), P("inp")),
        out_specs=P(None, "wide", "inp", None),
        check_vma=False,
    )
```

```python
import math

import jax
import jax.numpy as jnp
from jax import lax
from jax.sharding import PartitionSpec as P

AVG = 16


def passed_along(value, axis, steps):
    count = lax.axis_size(axis)
    initial, last = (max(0, -steps), min(count, count - steps))
    return lax.ppermute(value, axis, [(source, source + steps) for source in range(initial, last)])


def phase_tables(rows_count, cols_count, modulus):
    first_index = jnp.arange(rows_count, dtype=jnp.int32)[:, None]
    second_index = jnp.arange(cols_count, dtype=jnp.int32)[None, :]
    angle = (first_index * second_index % modulus).astype(jnp.float32) * (2.0 * math.pi / modulus)
    return (jnp.cos(angle), jnp.sin(angle))


def filter_frames(voltages, prototype):
    members, width_all = voltages.shape
    taps_count, span_len = prototype.shape
    frames_own = width_all // span_len
    samples = [voltages[:, f * span_len : (f + 1) * span_len].astype(jnp.float32) for f in range(frames_own)]
    near = []
    for f in range(frames_own):
        total = prototype[0][None, :] * samples[f]
        for tap_index in range(1, min(f, taps_count - 1) + 1):
            total = total + prototype[tap_index][None, :] * samples[f - tap_index]
        near.append(total)
    near = list(lax.optimization_barrier(tuple(near)))
    rows = []
    for f in range(frames_own):
        if f >= taps_count - 1:
            rows.append((near[f], None))
            continue
        partial_sum = jnp.zeros((members, span_len), jnp.float32)
        for tap_index in range(f + 1, taps_count):
            partial_sum = partial_sum + prototype[tap_index][None, :] * samples[frames_own + f - tap_index]
        rows.append((near[f], passed_along(partial_sum.astype(jnp.bfloat16), "wide", 1)))
    return rows


def transform_rows(filtered, channels):
    rows, span_len = filtered.shape
    inner_len = min(span_len, 128)
    outer_len = span_len // inner_len
    kept_count = channels // outer_len
    precise = lax.Precision.HIGH
    shaped = filtered.reshape(rows, outer_len, inner_len)
    cos_one, sin_one = phase_tables(outer_len, outer_len, outer_len)
    first = jnp.stack([cos_one, -sin_one])
    stage = jnp.einsum("qka,ran->qkrn", first, shaped, precision=precise)
    cos_two, sin_two = phase_tables(outer_len, inner_len, span_len)
    signs = jnp.array([1.0, -1.0], jnp.float32)[:, None, None, None]
    turned = stage * cos_two[None, :, None, :] + stage[::-1] * (signs * sin_two[None, :, None, :])
    cos_three, sin_three = phase_tables(kept_count, inner_len, inner_len)
    second = jnp.stack(
        [jnp.stack([cos_three, sin_three], axis=1), jnp.stack([-sin_three, cos_three], axis=1)]
    )
    out = jnp.einsum("pmqn,qkrn->pmkr", second, turned, precision=precise)
    return out.reshape(2, channels, rows)


def channelize(voltages, prototype, input_gain, usable):
    members = voltages.shape[0]
    span_len = prototype.shape[1]
    channels = span_len // 2
    filtered = filter_frames(voltages, prototype)
    outs = []
    for near, incoming in filtered:
        if incoming is not None:
            if outs:
                outs[-1], incoming = lax.optimization_barrier((outs[-1], incoming))
            near = near + incoming.astype(jnp.float32)
        outs.append(transform_rows(near, channels))
    factor = input_gain * usable.astype(jnp.float32) / math.sqrt(span_len)
    return jnp.concatenate([(one * factor).astype(jnp.bfloat16) for one in outs], axis=2)


def shards(voltages, prototype, input_gain, usable):
    members = voltages.shape[0]
    spectra = channelize(voltages, prototype, input_gain, usable)
    _, channels, rows = spectra.shape
    frames_own = rows // members
    n_inp = lax.axis_size("inp")
    n_wide = lax.axis_size("wide")
    n_dev = n_inp * n_wide
    group_width = channels // n_dev
    chunks = spectra.reshape(2, n_dev, group_width, rows).transpose(1, 0, 2, 3)
    arrived = lax.all_to_all(chunks, ("wide", "inp"), 0, 0, tiled=True)
    arrived = arrived.reshape(n_wide, n_inp, 2, group_width, rows)
    depth = n_wide * group_width * frames_own
    real_part, imag_part = (
        jnp.concatenate(
            [
                arrived[:, :, part, :, f * members : (f + 1) * members]
                .transpose(1, 3, 0, 2)
                .reshape(n_inp * members, n_wide * group_width)
                for f in range(frames_own)
            ],
            axis=1,
        )
        for part in range(2)
    )
    right = jnp.concatenate([real_part, imag_part], axis=1)
    left = jnp.stack([right, jnp.concatenate([imag_part, -real_part], axis=1)])
    normalize = 1.0 / math.sqrt(depth)
    left = left.reshape(2, n_inp, members, left.shape[-1]).transpose(1, 0, 2, 3)
    products = jnp.einsum("jpak,bk->jpab", left, right, preferred_element_type=jnp.float32) * normalize
    spread = lax.all_to_all(products, "inp", 0, 0, tiled=True)
    return spread.transpose(1, 0, 2, 3)


def solution(mesh):
    return jax.shard_map(
        shards,
        mesh=mesh,
        in_specs=(P("inp", "wide"), P(), P("inp"), P("inp")),
        out_specs=P(None, "wide", "inp", None),
        check_vma=False,
    )
```

```python
import math

import jax
import jax.numpy as jnp
from jax import lax
from jax.sharding import PartitionSpec as P

AVG = 16


def passed_along(value, axis, steps):
    count = lax.axis_size(axis)
    initial, last = (max(0, -steps), min(count, count - steps))
    return lax.ppermute(value, axis, [(source, source + steps) for source in range(initial, last)])


def phase_tables(rows_count, cols_count, modulus):
    first_index = jnp.arange(rows_count, dtype=jnp.int32)[:, None]
    second_index = jnp.arange(cols_count, dtype=jnp.int32)[None, :]
    angle = (first_index * second_index % modulus).astype(jnp.float32) * (2.0 * math.pi / modulus)
    return (jnp.cos(angle), jnp.sin(angle))


def filter_frames(voltages, prototype):
    members, width_all = voltages.shape
    taps_count, span_len = prototype.shape
    frames_own = width_all // span_len
    samples = [voltages[:, f * span_len : (f + 1) * span_len].astype(jnp.float32) for f in range(frames_own)]
    near = []
    for f in range(frames_own):
        total = prototype[0][None, :] * samples[f]
        for tap_index in range(1, min(f, taps_count - 1) + 1):
            total = total + prototype[tap_index][None, :] * samples[f - tap_index]
        near.append(total)
    inner_len = min(span_len, 128)
    near = [one.reshape(members, span_len // inner_len, inner_len) for one in near]
    near = [one.reshape(members, span_len) for one in lax.optimization_barrier(tuple(near))]
    rows = []
    for f in range(frames_own):
        if f >= taps_count - 1:
            rows.append((near[f], None))
            continue
        partial_sum = jnp.zeros((members, span_len), jnp.float32)
        for tap_index in range(f + 1, taps_count):
            partial_sum = partial_sum + prototype[tap_index][None, :] * samples[frames_own + f - tap_index]
        rows.append((near[f], passed_along(partial_sum.astype(jnp.bfloat16), "wide", 1)))
    return rows


def transform_rows(filtered, channels):
    rows, span_len = filtered.shape
    inner_len = min(span_len, 128)
    outer_len = span_len // inner_len
    kept_count = channels // outer_len
    precise = lax.Precision.HIGH
    shaped = filtered.reshape(rows, outer_len, inner_len)
    cos_one, sin_one = phase_tables(outer_len, outer_len, outer_len)
    first = jnp.stack([cos_one, -sin_one])
    stage = jnp.einsum("qka,ran->qkrn", first, shaped, precision=precise)
    cos_two, sin_two = phase_tables(outer_len, inner_len, span_len)
    signs = jnp.array([1.0, -1.0], jnp.float32)[:, None, None, None]
    turned = stage * cos_two[None, :, None, :] + stage[::-1] * (signs * sin_two[None, :, None, :])
    cos_three, sin_three = phase_tables(kept_count, inner_len, inner_len)
    second = jnp.stack(
        [jnp.stack([cos_three, sin_three], axis=1), jnp.stack([-sin_three, cos_three], axis=1)]
    )
    out = jnp.einsum("pmqn,qkrn->pmkr", second, turned, precision=precise)
    return out.reshape(2, channels, rows)


def channelize(voltages, prototype, input_gain, usable):
    members = voltages.shape[0]
    span_len = prototype.shape[1]
    channels = span_len // 2
    filtered = filter_frames(voltages, prototype)
    outs = []
    for near, incoming in filtered:
        if incoming is not None:
            if outs:
                outs[-1], incoming = lax.optimization_barrier((outs[-1], incoming))
            near = near + incoming.astype(jnp.float32)
        outs.append(transform_rows(near, channels))
    factor = input_gain * usable.astype(jnp.float32) / math.sqrt(span_len)
    return jnp.concatenate([(one * factor).astype(jnp.bfloat16) for one in outs], axis=2)


def shards(voltages, prototype, input_gain, usable):
    members = voltages.shape[0]
    spectra = channelize(voltages, prototype, input_gain, usable)
    _, channels, rows = spectra.shape
    frames_own = rows // members
    n_inp = lax.axis_size("inp")
    n_wide = lax.axis_size("wide")
    n_dev = n_inp * n_wide
    group_width = channels // n_dev
    chunks = spectra.reshape(2, n_dev, group_width, rows).transpose(1, 0, 2, 3)
    arrived = lax.all_to_all(chunks, ("wide", "inp"), 0, 0, tiled=True)
    arrived = arrived.reshape(n_wide, n_inp, 2, group_width, rows)
    depth = n_wide * group_width * frames_own
    real_part, imag_part = (
        jnp.concatenate(
            [
                arrived[:, :, part, :, f * members : (f + 1) * members]
                .transpose(1, 3, 0, 2)
                .reshape(n_inp * members, n_wide * group_width)
                for f in range(frames_own)
            ],
            axis=1,
        )
        for part in range(2)
    )
    right = jnp.concatenate([real_part, imag_part], axis=1)
    left = jnp.stack([right, jnp.concatenate([imag_part, -real_part], axis=1)])
    normalize = 1.0 / math.sqrt(depth)
    left = left.reshape(2, n_inp, members, left.shape[-1]).transpose(1, 0, 2, 3)
    products = jnp.einsum("jpak,bk->jpab", left, right, preferred_element_type=jnp.float32) * normalize
    spread = lax.all_to_all(products, "inp", 0, 0, tiled=True)
    return spread.transpose(1, 0, 2, 3)


def solution(mesh):
    return jax.shard_map(
        shards,
        mesh=mesh,
        in_specs=(P("inp", "wide"), P(), P("inp"), P("inp")),
        out_specs=P(None, "wide", "inp", None),
        check_vma=False,
    )
```

```python
import math

import jax
import jax.numpy as jnp
from jax import lax
from jax.sharding import PartitionSpec as P

AVG = 16


def passed_along(value, axis, steps):
    count = lax.axis_size(axis)
    initial, last = (max(0, -steps), min(count, count - steps))
    return lax.ppermute(value, axis, [(source, source + steps) for source in range(initial, last)])


def phase_tables(rows_count, cols_count, modulus):
    first_index = jnp.arange(rows_count, dtype=jnp.int32)[:, None]
    second_index = jnp.arange(cols_count, dtype=jnp.int32)[None, :]
    angle = (first_index * second_index % modulus).astype(jnp.float32) * (2.0 * math.pi / modulus)
    return (jnp.cos(angle), jnp.sin(angle))


def filter_frames(voltages, prototype):
    members, width_all = voltages.shape
    taps_count, span_len = prototype.shape
    frames_own = width_all // span_len
    samples = [voltages[:, f * span_len : (f + 1) * span_len].astype(jnp.float32) for f in range(frames_own)]
    near = []
    for f in range(frames_own):
        total = prototype[0][None, :] * samples[f]
        for tap_index in range(1, min(f, taps_count - 1) + 1):
            total = total + prototype[tap_index][None, :] * samples[f - tap_index]
        near.append(total)
    inner_len = min(span_len, 128)
    near = [one.reshape(members, span_len // inner_len, inner_len) for one in near]
    near = [one.reshape(members, span_len) for one in lax.optimization_barrier(tuple(near))]
    rows = []
    for f in range(frames_own):
        if f >= taps_count - 1:
            rows.append((near[f], None))
            continue
        partial_sum = jnp.zeros((members, span_len), jnp.float32)
        for tap_index in range(f + 1, taps_count):
            partial_sum = partial_sum + prototype[tap_index][None, :] * samples[frames_own + f - tap_index]
        shaped = partial_sum.astype(jnp.bfloat16).reshape(members, span_len // inner_len, inner_len)
        rows.append((near[f], passed_along(shaped, "wide", 1).reshape(members, span_len)))
    return rows


def transform_rows(filtered, channels):
    rows, span_len = filtered.shape
    inner_len = min(span_len, 128)
    outer_len = span_len // inner_len
    kept_count = channels // outer_len
    precise = lax.Precision.HIGH
    shaped = filtered.reshape(rows, outer_len, inner_len)
    cos_one, sin_one = phase_tables(outer_len, outer_len, outer_len)
    first = jnp.stack([cos_one, -sin_one])
    stage = jnp.einsum("qka,ran->qkrn", first, shaped, precision=precise)
    cos_two, sin_two = phase_tables(outer_len, inner_len, span_len)
    signs = jnp.array([1.0, -1.0], jnp.float32)[:, None, None, None]
    turned = stage * cos_two[None, :, None, :] + stage[::-1] * (signs * sin_two[None, :, None, :])
    cos_three, sin_three = phase_tables(kept_count, inner_len, inner_len)
    second = jnp.stack(
        [jnp.stack([cos_three, sin_three], axis=1), jnp.stack([-sin_three, cos_three], axis=1)]
    )
    out = jnp.einsum("pmqn,qkrn->pmkr", second, turned, precision=precise)
    return out.reshape(2, channels, rows)


def channelize(voltages, prototype, input_gain, usable):
    members = voltages.shape[0]
    span_len = prototype.shape[1]
    channels = span_len // 2
    filtered = filter_frames(voltages, prototype)
    outs = []
    for near, incoming in filtered:
        if incoming is not None:
            if outs:
                outs[-1], incoming = lax.optimization_barrier((outs[-1], incoming))
            near = near + incoming.astype(jnp.float32)
        outs.append(transform_rows(near, channels))
    factor = input_gain * usable.astype(jnp.float32) / math.sqrt(span_len)
    return jnp.concatenate([(one * factor).astype(jnp.bfloat16) for one in outs], axis=2)


def shards(voltages, prototype, input_gain, usable):
    members = voltages.shape[0]
    spectra = channelize(voltages, prototype, input_gain, usable)
    _, channels, rows = spectra.shape
    frames_own = rows // members
    n_inp = lax.axis_size("inp")
    n_wide = lax.axis_size("wide")
    n_dev = n_inp * n_wide
    group_width = channels // n_dev
    chunks = spectra.reshape(2, n_dev, group_width, rows).transpose(1, 0, 2, 3)
    arrived = lax.all_to_all(chunks, ("wide", "inp"), 0, 0, tiled=True)
    arrived = arrived.reshape(n_wide, n_inp, 2, group_width, rows)
    depth = n_wide * group_width * frames_own
    real_part, imag_part = (
        jnp.concatenate(
            [
                arrived[:, :, part, :, f * members : (f + 1) * members]
                .transpose(1, 3, 0, 2)
                .reshape(n_inp * members, n_wide * group_width)
                for f in range(frames_own)
            ],
            axis=1,
        )
        for part in range(2)
    )
    right = jnp.concatenate([real_part, imag_part], axis=1)
    left = jnp.stack([right, jnp.concatenate([imag_part, -real_part], axis=1)])
    normalize = 1.0 / math.sqrt(depth)
    left = left.reshape(2, n_inp, members, left.shape[-1]).transpose(1, 0, 2, 3)
    products = jnp.einsum("jpak,bk->jpab", left, right, preferred_element_type=jnp.float32) * normalize
    spread = lax.all_to_all(products, "inp", 0, 0, tiled=True)
    return spread.transpose(1, 0, 2, 3)


def solution(mesh):
    return jax.shard_map(
        shards,
        mesh=mesh,
        in_specs=(P("inp", "wide"), P(), P("inp"), P("inp")),
        out_specs=P(None, "wide", "inp", None),
        check_vma=False,
    )
```
